128 devices in a mesh: expert: 32 (over y, z, core), hidden: 4 (over x).
Axes of the slice: x: 4, y: 4, z: 4, core: 2. Of those that a mesh axis runs over, the one named last changes fastest.
Arguments:
- tokens: bfloat16 [2048, 7168], P('expert'), may hold values from -6 to 6
- expert_ids: int32 [2048, 8], replicated, may hold values from 0 to 31, all different within a row; in each aligned block of 64 rows (0 to 63, 64 to 127, ...) at most 24 rows name the same one
- gate_weight: bfloat16 [32, 7168, 2048], P('expert', None, 'hidden')
- up_weight: bfloat16 [32, 7168, 2048], P('expert', None, 'hidden')
Outputs:
- expert_hidden: bfloat16 [32, 32, 24, 2048], P('expert', None, None, 'hidden')
The draws below stay inside these ranges and needn't reach their ends.
Inputs may be any that keep to these rules, and one draw needn't show every extreme that they name: `expert_ids`: each row names 8 different experts; among the rows of one device no expert is named more than 24 times, and in every draw some expert is named exactly 24 times there.
All inputs are finite; a program needn't handle non-finite values.
Results may differ from the reference program's by a relative error of at most 0.0058.
Values may be sent and summed in bfloat16 or wider, within the bound.
No kernel may reach another device: no remote copies, remote signals or barrier semaphores. Data moves between devices by JAX's collectives and lax.ppermute only.
A program may use at most 192 MiB of HBM per device.

```python
import math
import jax
import jax.numpy as jnp
import numpy as np
from jax import lax

D = 7168
FF = 2048
TOPK = 8
EXPERTS = 32
SWEEPS = 5
TOK_DEV = 64
CAP = 24
TOKENS = 2048


def row_places(key):
    shared = jax.random.fold_in(key, 7)
    spread = jax.random.uniform(shared, (EXPERTS, D, 1), jnp.float32, 0.0, 1.0)
    return 8.0 * spread * spread


def weight_common(key, salt, reverse):
    places = row_places(key)
    key = jax.random.fold_in(key, salt)
    keys = jax.random.split(key, 5)
    base = jax.random.normal(keys[0], (EXPERTS, D, FF), jnp.float32)
    row_part = jnp.exp(jax.random.uniform(keys[1], (EXPERTS, D, 1), jnp.float32, 0.0, math.log(10.0)))
    col_part = jnp.exp(jax.random.uniform(keys[2], (EXPERTS, 1, FF), jnp.float32, 0.0, math.log(4.0)))
    rough = jnp.exp(math.log(16.0) * (jax.random.uniform(keys[3], (EXPERTS, D, FF), jnp.float32, 0.0, 1.0) - 0.5))
    block = (jnp.arange(FF, dtype=jnp.int32) // (FF // 4)).astype(jnp.float32)
    if reverse:
        block = 3.0 - block
    within = jax.random.uniform(keys[4], (EXPERTS, 1, FF), jnp.float32, 0.0, 1.0)
    col_places = 2.0 * block[None, None, :] + 2.0 * within
    band = jnp.exp(-1.2 * jnp.abs(places - col_places))
    values = base * row_part * col_part * rough * band / math.sqrt(D)
    return values.astype(jnp.bfloat16)


def draw_gate_weight(key, part):
    return weight_common(key, 11, False)


def draw_up_weight(key, part):
    return weight_common(key, 23, True)


def level_of(key, shape, cuts, least, top_value):
    def one(axis_at, shards_of):
        heights = jax.random.uniform(jax.random.fold_in(jax.random.fold_in(key, 6), axis_at), (shards_of,), jnp.float32, least / len(cuts), top_value / len(cuts))
        return jnp.repeat(jnp.exp(heights), shape[axis_at] // shards_of).reshape((-1,) + (1,) * (len(shape) - axis_at - 1))

    gain = one(*cuts[0])
    for cut in cuts[1:]:
        gain = gain * one(*cut)
    return gain


def deal_out(stream_key, own, number, rows, count, top, most, skew):
    order = jax.random.permutation(stream_key, count)
    heavy_load, ordinary = load_shares(count, rows * top, most, skew, True), load_shares(count, rows * top, most, skew, False)
    places = jnp.arange(count)

    def named(tallies, rotation):
        used = int((tallies > 0).sum())
        fixed = max(1, used // 4)
        passed = fixed + (places - fixed + rotation * (used - fixed)) % max(1, count - fixed)
        return jnp.zeros((count,), jnp.int32).at[order[jnp.where(places < fixed, places, passed)]].set(jnp.asarray(tallies, jnp.int32))

    tallies = jnp.where(number % 4 == 0, named(heavy_load, number // 4), named(ordinary, number - number // 4 - 1))
    mixed = jax.random.permutation(jax.random.fold_in(own, 3), count)
    donor, receiver = mixed[0:count // 2 * 2:2], mixed[1:count // 2 * 2:2]
    room = jnp.minimum(tallies[donor] - 1, most - tallies[receiver]) // 2
    room = jnp.where((donor == order[0]) | (receiver == order[0]) | (tallies[receiver] == 0), 0, jnp.maximum(room, 0))
    passed = jax.random.randint(jax.random.fold_in(own, 4), (count // 2,), 0, 1 << 20) % (room + 1)
    tallies = tallies.at[donor].add(-passed).at[receiver].add(passed)
    members = jnp.searchsorted(jnp.cumsum(tallies), jnp.arange(rows * top), side="right").astype(jnp.int32)
    table = members.reshape(top, rows).T
    table = table[jax.random.permutation(jax.random.fold_in(own, 1), rows)]
    rotation = jax.random.randint(jax.random.fold_in(own, 2), (rows, 1), 0, top)
    return jnp.take_along_axis(table, (jnp.arange(top)[None, :] + rotation) % top, axis=1)


def load_shares(amount, total, bound, lean, full):
    loads = [(1 << 20) // math.isqrt(standing ** lean) + 1 for standing in range(1, amount + 1)]
    largest = bound if full else min(bound, max(-(-total // amount), total * loads[0] // sum(loads)))
    least = 1 if total - largest >= amount - 1 else 0
    counts, rest = [largest] + [least] * (amount - 1), total - largest - least * (amount - 1)
    while rest > 0:
        free = [i for i in range(1, amount) if counts[i] < largest] or [i for i in range(1, amount) if counts[i] < bound]
        mass, remaining = sum([loads[i] for i in free]), rest
        for i in free:
            extra = min(bound - counts[i], max(1, remaining * loads[i] // mass), rest)
            counts[i] = counts[i] + extra
            rest = rest - extra
    return np.array(counts)


def scatter_about(own_key, dims, deviation, most, cuts=(), held_as=jnp.bfloat16):
    loudness = level_of(own_key, dims, cuts, -0.22, 0.18) if cuts else 1.0
    array = jax.random.normal(own_key, dims, jnp.float32) * deviation * loudness
    return jnp.minimum(jnp.maximum(array, -most), most).astype(held_as)


def setup_inputs(seed: int = 0) -> dict:
    splits = jax.random.split(jax.random.key(seed), 5)
    tokens = scatter_about(splits[0], (TOKENS, D), 1.0, 6.0, ((0, 32),))
    expert_ids_keys = jax.random.split(jax.random.fold_in(splits[1], 1), TOKENS // TOK_DEV)
    expert_ids_turns = jax.random.permutation(jax.random.fold_in(splits[1], 3), TOKENS // TOK_DEV)
    expert_ids = jax.vmap(lambda own, number: deal_out(jax.random.fold_in(splits[1], 2), own, number, TOK_DEV, EXPERTS, TOPK, CAP, 2))(expert_ids_keys, expert_ids_turns).reshape((TOKENS, TOPK))
    gate_weight = draw_gate_weight(jax.random.fold_in(splits[4], 71), 0)
    up_weight = draw_up_weight(jax.random.fold_in(splits[4], 71), 0)
    return {"tokens": tokens, "expert_ids": expert_ids, "gate_weight": gate_weight, "up_weight": up_weight}


EPS = 1e-06

def slot_table(block_ids):
    flat_ids = block_ids.reshape(-1)
    onehot = (flat_ids[:, None] == jnp.arange(EXPERTS, dtype=jnp.int32)[None, :]).astype(jnp.int32)
    before = jnp.cumsum(onehot, axis=0) - onehot
    my_rank = lax.optimization_barrier(jnp.sum(before * onehot, axis=1))
    token_index = (jnp.arange(flat_ids.shape[0], dtype=jnp.int32) // TOPK).astype(jnp.int32)
    position = flat_ids * CAP + my_rank
    filled = jnp.full((EXPERTS * CAP,), TOK_DEV, jnp.int32).at[position].set(token_index)
    return filled.reshape(EXPERTS, CAP)

def equilibrate(gate_w, up_w):
    gate_f = gate_w.astype(jnp.float32)
    up_f = up_w.astype(jnp.float32)
    gate_sq = gate_f * gate_f
    up_sq = up_f * up_f
    gate_cols = jnp.ones((FF,), jnp.float32)
    up_cols = jnp.ones((FF,), jnp.float32)
    high = lax.Precision.HIGHEST
    for sweep in range(SWEEPS):
        row_sums = jnp.dot(gate_sq, gate_cols * gate_cols, precision=high) + jnp.dot(up_sq, up_cols * up_cols, precision=high)
        row_scale = lax.rsqrt(D * row_sums / (2 * FF) + EPS)
        gate_cols = lax.rsqrt(jnp.dot(row_scale * row_scale, gate_sq, precision=high) + EPS)
        up_cols = lax.rsqrt(jnp.dot(row_scale * row_scale, up_sq, precision=high) + EPS)
    gate_eq = (gate_f * row_scale[:, None] * gate_cols[None, :]).astype(jnp.bfloat16)
    up_eq = (up_f * row_scale[:, None] * up_cols[None, :]).astype(jnp.bfloat16)
    return (gate_eq, up_eq)

def reference(tokens, expert_ids, gate_weight, up_weight):
    sources = TOKENS // TOK_DEV
    tables = jax.vmap(slot_table)(expert_ids.reshape(sources, TOK_DEV, TOPK))
    offsets = (jnp.arange(sources, dtype=jnp.int32) * TOK_DEV)[:, None, None]
    global_index = jnp.where(tables == TOK_DEV, TOKENS, tables + offsets).astype(jnp.int32)
    global_index = jnp.transpose(global_index, (1, 0, 2))
    padded = jnp.concatenate([tokens, jnp.zeros((1, D), jnp.bfloat16)], axis=0)

    def one_expert(operands):
        gate_w, up_w, index_block = operands
        gate_eq, up_eq = equilibrate(gate_w, up_w)
        gathered = padded[index_block.reshape(-1)]
        gate_act = jnp.dot(gathered, gate_eq, preferred_element_type=jnp.float32)
        up_act = jnp.dot(gathered, up_eq, preferred_element_type=jnp.float32)
        result = (jax.nn.silu(gate_act) * up_act).astype(jnp.bfloat16)
        return result.reshape(sources, CAP, FF)
    return lax.map(one_expert, (gate_weight, up_weight, global_index))
```

```python
import jax
import jax.numpy as jnp
from jax import lax
from jax.sharding import PartitionSpec as P

TOPK = 8
EXPERTS = 32
SWEEPS = 5
TOK_DEV = 64
CAP = 24
COL_GROUPS = 56
HANDOFF = 2


EPS = 1e-06


def dispatch_rows(block_ids, tokens, first_slot, slots):
    tok_local, topk = block_ids.shape
    flat_ids = block_ids.reshape(-1)
    onehot = (flat_ids[:, None] == jnp.arange(EXPERTS, dtype=jnp.int32)[None, :]).astype(jnp.int32)
    before = jnp.cumsum(onehot, axis=0) - onehot
    my_rank = jnp.sum(before * onehot, axis=1) - first_slot
    pair_ids = flat_ids.reshape(tok_local, topk)
    pair_rank = my_rank.reshape(tok_local, topk)
    hit = (pair_ids[None, None] == jnp.arange(EXPERTS, dtype=jnp.int32)[:, None, None, None]) & (
        pair_rank[None, None] == jnp.arange(slots, dtype=jnp.int32)[None, :, None, None]
    )
    select = jnp.any(hit, axis=3).astype(tokens.dtype).reshape(EXPERTS * slots, tok_local)
    rows = jnp.dot(select, tokens, preferred_element_type=jnp.float32).astype(tokens.dtype)
    return rows.reshape(EXPERTS, 1, slots, tokens.shape[1])


def hidden_sum(values):
    n = lax.axis_size("hidden")
    total = values
    for shift in range(1, n):
        total = total + lax.ppermute(values, "hidden", [(i, (i + shift) % n) for i in range(n)])
    return total


def row_terms(weight, cols_sq):
    values = weight.astype(jnp.float32)
    return jnp.sum(values * values * cols_sq[:, None, :], axis=2)


def col_terms(weight, scale_sq):
    values = weight.astype(jnp.float32)
    terms = values * values * scale_sq[:, :, None]
    exp_local, width, ff_local = terms.shape
    grouped = jnp.sum(terms.reshape(exp_local, COL_GROUPS, width // COL_GROUPS, ff_local), axis=1)
    grouped = lax.optimization_barrier(grouped)
    return jnp.sum(grouped, axis=1)


def shards(tokens, expert_ids, gate_weight, up_weight):
    exp_local = gate_weight.shape[0]
    width = gate_weight.shape[1]
    ff_local = gate_weight.shape[2]
    n_hidden = lax.axis_size("hidden")
    ff_total = ff_local * n_hidden
    my_index = lax.axis_index("expert")
    parity = lax.axis_index("hidden") % 2
    half = CAP // 2

    tok_local = tokens.shape[0]
    block_ids = lax.dynamic_slice_in_dim(expert_ids, my_index * tok_local, tok_local, 0)
    chunk = half // 2
    sends = [dispatch_rows(block_ids, tokens, parity * half + c * chunk, chunk) for c in range(2)]
    sends, gate_weight, up_weight = lax.optimization_barrier((sends, gate_weight, up_weight))
    down = [(i, (i - 1) % n_hidden) for i in range(n_hidden)]
    up = [(i, (i + 1) % n_hidden) for i in range(n_hidden)]

    def exchange(rows):
        split = rows.shape[2] // 2
        from_next = lax.ppermute(rows[:, :, :split], "hidden", down)
        from_prev = lax.ppermute(rows[:, :, split:], "hidden", up)
        return jnp.concatenate([from_next, from_prev], axis=2)

    mine = [lax.all_to_all(sends[0], "expert", split_axis=0, concat_axis=1, tiled=True)]
    other = []

    gate_cols = jnp.ones((exp_local, ff_local), jnp.float32)
    up_cols = jnp.ones((exp_local, ff_local), jnp.float32)
    for sweep in range(SWEEPS):
        if sweep == HANDOFF:
            first, later, gate_cols, up_cols = lax.optimization_barrier(
                (mine[0], sends[1], gate_cols, up_cols)
            )
            mine = [first, lax.all_to_all(later, "expert", split_axis=0, concat_axis=1, tiled=True)]
            other.append(exchange(first))
        partial_rows = row_terms(gate_weight, gate_cols * gate_cols) + row_terms(
            up_weight, up_cols * up_cols
        )
        row_sums = hidden_sum(partial_rows)
        row_scale = lax.rsqrt(width * row_sums / (2 * ff_total) + EPS)
        scale_sq = row_scale * row_scale
        gate_cols = lax.rsqrt(col_terms(gate_weight, scale_sq) + EPS)
        up_cols = lax.rsqrt(col_terms(up_weight, scale_sq) + EPS)
    other.append(exchange(mine[1]))
    mine = jnp.concatenate(mine, axis=2)
    other = jnp.concatenate(other, axis=2)
    gate_eq = (
        gate_weight.astype(jnp.float32) * row_scale[:, :, None] * gate_cols[:, None, :]
    ).astype(jnp.bfloat16)
    up_eq = (up_weight.astype(jnp.float32) * row_scale[:, :, None] * up_cols[:, None, :]).astype(
        jnp.bfloat16
    )

    def expert_mlp(rows):
        gate_act = jnp.einsum("ensd,edf->ensf", rows, gate_eq, preferred_element_type=jnp.float32)
        up_act = jnp.einsum("ensd,edf->ensf", rows, up_eq, preferred_element_type=jnp.float32)
        return (jax.nn.silu(gate_act) * up_act).astype(jnp.bfloat16)

    res_mine = expert_mlp(mine)
    res_other = expert_mlp(other)
    low = jnp.where(parity == 0, res_mine, res_other)
    high = jnp.where(parity == 0, res_other, res_mine)
    return jnp.concatenate([low, high], axis=2)


def solution(mesh):
    in_specs = (P("expert", None), P(), P("expert", None, "hidden"), P("expert", None, "hidden"))
    out_specs = P("expert", None, None, "hidden")
    return jax.shard_map(shards, mesh=mesh, in_specs=in_specs, out_specs=out_specs, check_vma=False)
```

```python
import jax
import jax.numpy as jnp
from jax import lax
from jax.sharding import PartitionSpec as P

TOPK = 8
EXPERTS = 32
SWEEPS = 5
TOK_DEV = 64
CAP = 24
HANDOFF = 2


EPS = 1e-06


def dispatch_rows(block_ids, tokens, first_slot, slots):
    tok_local, topk = block_ids.shape
    flat_ids = block_ids.reshape(-1)
    onehot = (flat_ids[:, None] == jnp.arange(EXPERTS, dtype=jnp.int32)[None, :]).astype(jnp.int32)
    before = jnp.cumsum(onehot, axis=0) - onehot
    my_rank = jnp.sum(before * onehot, axis=1) - first_slot
    pair_ids = flat_ids.reshape(tok_local, topk)
    pair_rank = my_rank.reshape(tok_local, topk)
    hit = (pair_ids[None, None] == jnp.arange(EXPERTS, dtype=jnp.int32)[:, None, None, None]) & (
        pair_rank[None, None] == jnp.arange(slots, dtype=jnp.int32)[None, :, None, None]
    )
    select = jnp.any(hit, axis=3).astype(tokens.dtype)
    rows = jnp.einsum("est,td->esd", select, tokens, preferred_element_type=jnp.float32)
    return rows.astype(tokens.dtype)[:, None]


def hidden_sum(values):
    n = lax.axis_size("hidden")
    total = values
    for shift in range(1, n):
        total = total + lax.ppermute(values, "hidden", [(i, (i + shift) % n) for i in range(n)])
    return total


def row_terms(weight, cols_sq):
    values = weight.astype(jnp.float32)
    return jnp.sum(values * values * cols_sq[:, None, :], axis=2)


def col_terms(weight, scale_sq):
    values = weight.astype(jnp.float32)
    return jnp.sum(values * values * scale_sq[:, :, None], axis=1)


def shards(tokens, expert_ids, gate_weight, up_weight):
    exp_local = gate_weight.shape[0]
    width = gate_weight.shape[1]
    ff_local = gate_weight.shape[2]
    n_hidden = lax.axis_size("hidden")
    ff_total = ff_local * n_hidden
    my_index = lax.axis_index("expert")
    parity = lax.axis_index("hidden") % 2
    half = CAP // 2

    tok_local = tokens.shape[0]
    block_ids = lax.dynamic_slice_in_dim(expert_ids, my_index * tok_local, tok_local, 0)
    outgoing = dispatch_rows(block_ids, tokens, parity * half, half)
    mine = lax.all_to_all(outgoing, "expert", split_axis=0, concat_axis=1, tiled=True)

    def sweep(_, carry):
        gate_cols, up_cols, _ = carry
        partial_rows = row_terms(gate_weight, gate_cols * gate_cols) + row_terms(
            up_weight, up_cols * up_cols
        )
        row_sums = hidden_sum(partial_rows)
        row_scale = lax.rsqrt(width * row_sums / (2 * ff_total) + EPS)
        scale_sq = row_scale * row_scale
        gate_cols = lax.rsqrt(col_terms(gate_weight, scale_sq) + EPS)
        up_cols = lax.rsqrt(col_terms(up_weight, scale_sq) + EPS)
        return gate_cols, up_cols, row_scale

    carry = (
        jnp.ones((exp_local, ff_local), jnp.float32),
        jnp.ones((exp_local, ff_local), jnp.float32),
        jnp.ones((exp_local, width), jnp.float32),
    )
    for step in range(HANDOFF):
        carry = sweep(step, carry)
    mine, carry = lax.optimization_barrier((mine, carry))
    quarter = half // 2
    from_next = lax.ppermute(
        mine[:, :, :quarter], "hidden", [(i, (i - 1) % n_hidden) for i in range(n_hidden)]
    )
    from_prev = lax.ppermute(
        mine[:, :, quarter:], "hidden", [(i, (i + 1) % n_hidden) for i in range(n_hidden)]
    )
    other = jnp.concatenate([from_next, from_prev], axis=2)
    gate_cols, up_cols, row_scale = lax.fori_loop(HANDOFF, SWEEPS, sweep, carry)
    gate_eq = (
        gate_weight.astype(jnp.float32) * row_scale[:, :, None] * gate_cols[:, None, :]
    ).astype(jnp.bfloat16)
    up_eq = (up_weight.astype(jnp.float32) * row_scale[:, :, None] * up_cols[:, None, :]).astype(
        jnp.bfloat16
    )

    def expert_mlp(rows):
        gate_act = jnp.einsum("ensd,edf->ensf", rows, gate_eq, preferred_element_type=jnp.float32)
        up_act = jnp.einsum("ensd,edf->ensf", rows, up_eq, preferred_element_type=jnp.float32)
        return (jax.nn.silu(gate_act) * up_act).astype(jnp.bfloat16)

    res_mine = expert_mlp(mine)
    res_other = expert_mlp(other)
    low = jnp.where(parity == 0, res_mine, res_other)
    high = jnp.where(parity == 0, res_other, res_mine)
    return jnp.concatenate([low, high], axis=2)


def solution(mesh):
    in_specs = (P("expert", None), P(), P("expert", None, "hidden"), P("expert", None, "hidden"))
    out_specs = P("expert", None, None, "hidden")
    return jax.shard_map(shards, mesh=mesh, in_specs=in_specs, out_specs=out_specs, check_vma=False)
```

```python
import jax
import jax.numpy as jnp
from jax import lax
from jax.sharding import PartitionSpec as P

TOPK = 8
EXPERTS = 32
SWEEPS = 5
TOK_DEV = 64
CAP = 24


EPS = 1e-06


def dispatch_rows(block_ids, tokens):
    tok_local, topk = block_ids.shape
    flat_ids = block_ids.reshape(-1)
    onehot = (flat_ids[:, None] == jnp.arange(EXPERTS, dtype=jnp.int32)[None, :]).astype(jnp.int32)
    before = jnp.cumsum(onehot, axis=0) - onehot
    my_rank = jnp.sum(before * onehot, axis=1)
    pair_ids = flat_ids.reshape(tok_local, topk)
    pair_rank = my_rank.reshape(tok_local, topk)
    hit = (pair_ids[None, None] == jnp.arange(EXPERTS, dtype=jnp.int32)[:, None, None, None]) & (
        pair_rank[None, None] == jnp.arange(CAP, dtype=jnp.int32)[None, :, None, None]
    )
    select = jnp.any(hit, axis=3).astype(tokens.dtype)
    rows = jnp.einsum("est,td->esd", select, tokens, preferred_element_type=jnp.float32)
    return rows.astype(tokens.dtype)[:, None]


def hidden_sum(values):
    n = lax.axis_size("hidden")
    total = values
    for shift in range(1, n):
        total = total + lax.ppermute(values, "hidden", [(i, (i + shift) % n) for i in range(n)])
    return total


def row_terms(weight, cols_sq):
    values = weight.astype(jnp.float32)
    return jnp.sum(values * values * cols_sq[:, None, :], axis=2)


def col_terms(weight, scale_sq):
    values = weight.astype(jnp.float32)
    return jnp.sum(values * values * scale_sq[:, :, None], axis=1)


def shards(tokens, expert_ids, gate_weight, up_weight):
    exp_local = gate_weight.shape[0]
    width = gate_weight.shape[1]
    ff_local = gate_weight.shape[2]
    ff_total = ff_local * lax.axis_size("hidden")
    my_index = lax.axis_index("expert")
    tok_local = tokens.shape[0]
    block_ids = lax.dynamic_slice_in_dim(expert_ids, my_index * tok_local, tok_local, 0)
    outgoing = dispatch_rows(block_ids, tokens)
    routed = lax.all_to_all(outgoing, "expert", split_axis=0, concat_axis=1, tiled=True)
    def sweep(_, carry):
        gate_cols, up_cols, _ = carry
        partial_rows = row_terms(gate_weight, gate_cols * gate_cols) + row_terms(
            up_weight, up_cols * up_cols
        )
        row_sums = hidden_sum(partial_rows)
        row_scale = lax.rsqrt(width * row_sums / (2 * ff_total) + EPS)
        scale_sq = row_scale * row_scale
        gate_cols = lax.rsqrt(col_terms(gate_weight, scale_sq) + EPS)
        up_cols = lax.rsqrt(col_terms(up_weight, scale_sq) + EPS)
        return gate_cols, up_cols, row_scale

    carry = (
        jnp.ones((exp_local, ff_local), jnp.float32),
        jnp.ones((exp_local, ff_local), jnp.float32),
        jnp.ones((exp_local, width), jnp.float32),
    )
    gate_cols, up_cols, row_scale = lax.fori_loop(0, SWEEPS, sweep, carry)
    gate_eq = (
        gate_weight.astype(jnp.float32) * row_scale[:, :, None] * gate_cols[:, None, :]
    ).astype(jnp.bfloat16)
    up_eq = (up_weight.astype(jnp.float32) * row_scale[:, :, None] * up_cols[:, None, :]).astype(
        jnp.bfloat16
    )
    gate_act = jnp.einsum("ensd,edf->ensf", routed, gate_eq, preferred_element_type=jnp.float32)
    up_act = jnp.einsum("ensd,edf->ensf", routed, up_eq, preferred_element_type=jnp.float32)
    return (jax.nn.silu(gate_act) * up_act).astype(jnp.bfloat16)


def solution(mesh):
    in_specs = (P("expert", None), P(), P("expert", None, "hidden"), P("expert", None, "hidden"))
    out_specs = P("expert", None, None, "hidden")
    return jax.shard_map(shards, mesh=mesh, in_specs=in_specs, out_specs=out_specs, check_vma=False)
```

```python
import jax
import jax.numpy as jnp
from jax import lax
from jax.sharding import PartitionSpec as P

TOPK = 8
EXPERTS = 32
SWEEPS = 5
TOK_DEV = 64
CAP = 24


EPS = 1e-06


def dispatch_rows(block_ids, tokens):
    tok_local, topk = block_ids.shape
    flat_ids = block_ids.reshape(-1)
    onehot = (flat_ids[:, None] == jnp.arange(EXPERTS, dtype=jnp.int32)[None, :]).astype(jnp.int32)
    before = jnp.cumsum(onehot, axis=0) - onehot
    my_rank = jnp.sum(before * onehot, axis=1)
    pair_ids = flat_ids.reshape(tok_local, topk)
    pair_rank = my_rank.reshape(tok_local, topk)
    hit = (pair_ids[None, None] == jnp.arange(EXPERTS, dtype=jnp.int32)[:, None, None, None]) & (
        pair_rank[None, None] == jnp.arange(CAP, dtype=jnp.int32)[None, :, None, None]
    )
    select = jnp.any(hit, axis=3).astype(tokens.dtype)
    rows = jnp.einsum("est,td->esd", select, tokens, preferred_element_type=jnp.float32)
    return rows.astype(tokens.dtype)[:, None]


def hidden_sum(values):
    n = lax.axis_size("hidden")
    total = values
    for shift in range(1, n):
        total = total + lax.ppermute(values, "hidden", [(i, (i + shift) % n) for i in range(n)])
    return total


def row_terms(weight, cols_sq):
    values = weight.astype(jnp.float32)
    return jnp.sum(values * values * cols_sq[:, None, :], axis=2)


def col_terms(weight, scale_sq):
    values = weight.astype(jnp.float32)
    return jnp.sum(values * values * scale_sq[:, :, None], axis=1)


def shards(tokens, expert_ids, gate_weight, up_weight):
    exp_local = gate_weight.shape[0]
    width = gate_weight.shape[1]
    ff_local = gate_weight.shape[2]
    ff_total = ff_local * lax.axis_size("hidden")
    my_index = lax.axis_index("expert")
    tok_local = tokens.shape[0]
    block_ids = lax.dynamic_slice_in_dim(expert_ids, my_index * tok_local, tok_local, 0)
    outgoing = dispatch_rows(block_ids, tokens)
    routed = lax.all_to_all(outgoing, "expert", split_axis=0, concat_axis=1, tiled=True)
    def sweep(_, carry):
        gate_cols, up_cols, _ = carry
        partial_rows = row_terms(gate_weight, gate_cols * gate_cols) + row_terms(
            up_weight, up_cols * up_cols
        )
        row_sums = hidden_sum(partial_rows)
        row_scale = lax.rsqrt(width * row_sums / (2 * ff_total) + EPS)
        scale_sq = row_scale * row_scale
        gate_cols = lax.rsqrt(col_terms(gate_weight, scale_sq) + EPS)
        up_cols = lax.rsqrt(col_terms(up_weight, scale_sq) + EPS)
        return gate_cols, up_cols, row_scale

    carry = (
        jnp.ones((exp_local, ff_local), jnp.float32),
        jnp.ones((exp_local, ff_local), jnp.float32),
        jnp.ones((exp_local, width), jnp.float32),
    )
    gate_cols, up_cols, row_scale = lax.fori_loop(0, SWEEPS, sweep, carry)
    gate_eq = (
        gate_weight.astype(jnp.float32) * row_scale[:, :, None] * gate_cols[:, None, :]
    ).astype(jnp.bfloat16)
    up_eq = (up_weight.astype(jnp.float32) * row_scale[:, :, None] * up_cols[:, None, :]).astype(
        jnp.bfloat16
    )
    both_eq = lax.optimization_barrier(jnp.concatenate([gate_eq, up_eq], axis=2))
    act = jnp.einsum("ensd,edf->ensf", routed, both_eq, preferred_element_type=jnp.float32)
    gate_act = act[..., :ff_local]
    up_act = act[..., ff_local:]
    return (jax.nn.silu(gate_act) * up_act).astype(jnp.bfloat16)


def solution(mesh):
    in_specs = (P("expert", None), P(), P("expert", None, "hidden"), P("expert", None, "hidden"))
    out_specs = P("expert", None, None, "hidden")
    return jax.shard_map(shards, mesh=mesh, in_specs=in_specs, out_specs=out_specs, check_vma=False)
```

```python
import jax
import jax.numpy as jnp
from jax import lax
from jax.experimental import pallas as pl
from jax.experimental.pallas import tpu as pltpu
from jax.sharding import PartitionSpec as P

TOPK = 8
EXPERTS = 32
SWEEPS = 5
TOK_DEV = 64
CAP = 24


EPS = 1e-06
K_TILE = 1024


def gated_body(rows_ref, gate_ref, up_ref, out_ref, gate_acc, up_acc):
    step = pl.program_id(0)

    @pl.when(step == 0)
    def _():
        gate_acc[...] = jnp.zeros_like(gate_acc)
        up_acc[...] = jnp.zeros_like(up_acc)

    rows = rows_ref[...]
    gate_acc[...] += jnp.dot(rows, gate_ref[...], preferred_element_type=jnp.float32)
    up_acc[...] += jnp.dot(rows, up_ref[...], preferred_element_type=jnp.float32)

    @pl.when(step == pl.num_programs(0) - 1)
    def _():
        g = gate_acc[...]
        out_ref[...] = (g / (1.0 + jnp.exp(-g)) * up_acc[...]).astype(out_ref.dtype)


def gated_matmul(rows, both, ff_local):
    m, width = rows.shape
    steps = width // K_TILE
    return pl.pallas_call(
        gated_body,
        grid=(steps,),
        in_specs=[
            pl.BlockSpec((m, K_TILE), lambda k: (0, k)),
            pl.BlockSpec((K_TILE, ff_local), lambda k: (k, 0)),
            pl.BlockSpec((K_TILE, ff_local), lambda k: (k, 1)),
        ],
        out_specs=pl.BlockSpec((m, ff_local), lambda k: (0, 0)),
        out_shape=jax.ShapeDtypeStruct((m, ff_local), jnp.bfloat16),
        scratch_shapes=[pltpu.VMEM((m, ff_local), jnp.float32), pltpu.VMEM((m, ff_local), jnp.float32)],
        compiler_params=pltpu.CompilerParams(dimension_semantics=("arbitrary",)),
        cost_estimate=pl.CostEstimate(
            flops=2 * m * width * 2 * ff_local,
            transcendentals=m * ff_local,
            bytes_accessed=2 * (m * width + width * 2 * ff_local + m * ff_local),
        ),
    )(rows, both, both)


def dispatch_rows(block_ids, tokens):
    tok_local, topk = block_ids.shape
    flat_ids = block_ids.reshape(-1)
    onehot = (flat_ids[:, None] == jnp.arange(EXPERTS, dtype=jnp.int32)[None, :]).astype(jnp.int32)
    before = jnp.cumsum(onehot, axis=0) - onehot
    my_rank = jnp.sum(before * onehot, axis=1)
    pair_ids = flat_ids.reshape(tok_local, topk)
    pair_rank = my_rank.reshape(tok_local, topk)
    hit = (pair_ids[None, None] == jnp.arange(EXPERTS, dtype=jnp.int32)[:, None, None, None]) & (
        pair_rank[None, None] == jnp.arange(CAP, dtype=jnp.int32)[None, :, None, None]
    )
    select = jnp.any(hit, axis=3).astype(tokens.dtype)
    rows = jnp.einsum("est,td->esd", select, tokens, preferred_element_type=jnp.float32)
    return rows.astype(tokens.dtype)[:, None]


def hidden_sum(values):
    n = lax.axis_size("hidden")
    total = values
    for shift in range(1, n):
        total = total + lax.ppermute(values, "hidden", [(i, (i + shift) % n) for i in range(n)])
    return total


def row_terms(weight, cols_sq):
    values = weight.astype(jnp.float32)
    return jnp.sum(values * values * cols_sq[:, None, :], axis=2)


def col_terms(weight, scale_sq):
    values = weight.astype(jnp.float32)
    return jnp.sum(values * values * scale_sq[:, :, None], axis=1)


def shards(tokens, expert_ids, gate_weight, up_weight):
    exp_local = gate_weight.shape[0]
    width = gate_weight.shape[1]
    ff_local = gate_weight.shape[2]
    ff_total = ff_local * lax.axis_size("hidden")
    my_index = lax.axis_index("expert")
    tok_local = tokens.shape[0]
    block_ids = lax.dynamic_slice_in_dim(expert_ids, my_index * tok_local, tok_local, 0)
    outgoing = dispatch_rows(block_ids, tokens)
    routed = lax.all_to_all(outgoing, "expert", split_axis=0, concat_axis=1, tiled=True)
    def sweep(_, carry):
        gate_cols, up_cols, _ = carry
        partial_rows = row_terms(gate_weight, gate_cols * gate_cols) + row_terms(
            up_weight, up_cols * up_cols
        )
        row_sums = hidden_sum(partial_rows)
        row_scale = lax.rsqrt(width * row_sums / (2 * ff_total) + EPS)
        scale_sq = row_scale * row_scale
        gate_cols = lax.rsqrt(col_terms(gate_weight, scale_sq) + EPS)
        up_cols = lax.rsqrt(col_terms(up_weight, scale_sq) + EPS)
        return gate_cols, up_cols, row_scale

    carry = (
        jnp.ones((exp_local, ff_local), jnp.float32),
        jnp.ones((exp_local, ff_local), jnp.float32),
        jnp.ones((exp_local, width), jnp.float32),
    )
    gate_cols, up_cols, row_scale = lax.fori_loop(0, SWEEPS, sweep, carry)
    gate_eq = (
        gate_weight.astype(jnp.float32) * row_scale[:, :, None] * gate_cols[:, None, :]
    ).astype(jnp.bfloat16)
    up_eq = (up_weight.astype(jnp.float32) * row_scale[:, :, None] * up_cols[:, None, :]).astype(
        jnp.bfloat16
    )
    both_eq = lax.optimization_barrier(jnp.concatenate([gate_eq, up_eq], axis=2))
    rows = routed.reshape(-1, width)
    hidden = gated_matmul(rows, both_eq.reshape(width, 2 * ff_local), ff_local)
    return hidden.reshape(routed.shape[:3] + (ff_local,))


def solution(mesh):
    in_specs = (P("expert", None), P(), P("expert", None, "hidden"), P("expert", None, "hidden"))
    out_specs = P("expert", None, None, "hidden")
    return jax.shard_map(shards, mesh=mesh, in_specs=in_specs, out_specs=out_specs, check_vma=False)
```

```python
import jax
import jax.numpy as jnp
from jax import lax
from jax.sharding import PartitionSpec as P

TOPK = 8
EXPERTS = 32
SWEEPS = 5
TOK_DEV = 64
CAP = 24


EPS = 1e-06


def dispatch_rows(block_ids, tokens):
    tok_local, topk = block_ids.shape
    flat_ids = block_ids.reshape(-1)
    pairs = flat_ids.shape[0]
    onehot = (flat_ids[:, None] == jnp.arange(EXPERTS, dtype=jnp.int32)[None, :]).astype(jnp.bfloat16)
    earlier = (
        jnp.arange(pairs, dtype=jnp.int32)[:, None] > jnp.arange(pairs, dtype=jnp.int32)[None, :]
    ).astype(jnp.bfloat16)
    before = jnp.dot(earlier, onehot, preferred_element_type=jnp.float32)
    my_rank = jnp.sum(before * onehot.astype(jnp.float32), axis=1).astype(jnp.int32)
    pair_ids = flat_ids.reshape(tok_local, topk)
    pair_rank = my_rank.reshape(tok_local, topk)
    hit = (pair_ids[None, None] == jnp.arange(EXPERTS, dtype=jnp.int32)[:, None, None, None]) & (
        pair_rank[None, None] == jnp.arange(CAP, dtype=jnp.int32)[None, :, None, None]
    )
    select = jnp.any(hit, axis=3).astype(tokens.dtype)
    rows = jnp.einsum("est,td->esd", select, tokens, preferred_element_type=jnp.float32)
    return rows.astype(tokens.dtype)[:, None]


def hidden_sum(values):
    n = lax.axis_size("hidden")
    total = values
    for shift in range(1, n):
        total = total + lax.ppermute(values, "hidden", [(i, (i + shift) % n) for i in range(n)])
    return total


def row_terms(weight, cols_sq):
    values = weight.astype(jnp.float32)
    return jnp.sum(values * values * cols_sq[:, None, :], axis=2)


def col_terms(weight, scale_sq):
    values = weight.astype(jnp.float32)
    return jnp.sum(values * values * scale_sq[:, :, None], axis=1)


def shards(tokens, expert_ids, gate_weight, up_weight):
    exp_local = gate_weight.shape[0]
    width = gate_weight.shape[1]
    ff_local = gate_weight.shape[2]
    ff_total = ff_local * lax.axis_size("hidden")
    my_index = lax.axis_index("expert")
    tok_local = tokens.shape[0]
    block_ids = lax.dynamic_slice_in_dim(expert_ids, my_index * tok_local, tok_local, 0)
    outgoing = dispatch_rows(block_ids, tokens)
    routed = lax.all_to_all(outgoing, "expert", split_axis=0, concat_axis=1, tiled=True)
    def sweep(_, carry):
        gate_cols, up_cols, _ = carry
        partial_rows = row_terms(gate_weight, gate_cols * gate_cols) + row_terms(
            up_weight, up_cols * up_cols
        )
        row_sums = hidden_sum(partial_rows)
        row_scale = lax.rsqrt(width * row_sums / (2 * ff_total) + EPS)
        scale_sq = row_scale * row_scale
        gate_cols = lax.rsqrt(col_terms(gate_weight, scale_sq) + EPS)
        up_cols = lax.rsqrt(col_terms(up_weight, scale_sq) + EPS)
        return gate_cols, up_cols, row_scale

    carry = (
        jnp.ones((exp_local, ff_local), jnp.float32),
        jnp.ones((exp_local, ff_local), jnp.float32),
        jnp.ones((exp_local, width), jnp.float32),
    )
    gate_cols, up_cols, row_scale = lax.fori_loop(0, SWEEPS, sweep, carry)
    gate_eq = (
        gate_weight.astype(jnp.float32) * row_scale[:, :, None] * gate_cols[:, None, :]
    ).astype(jnp.bfloat16)
    up_eq = (up_weight.astype(jnp.float32) * row_scale[:, :, None] * up_cols[:, None, :]).astype(
        jnp.bfloat16
    )
    both_eq = lax.optimization_barrier(jnp.concatenate([gate_eq, up_eq], axis=2))
    act = jnp.einsum("ensd,edf->ensf", routed, both_eq, preferred_element_type=jnp.float32)
    gate_act = act[..., :ff_local]
    up_act = act[..., ff_local:]
    return (jax.nn.silu(gate_act) * up_act).astype(jnp.bfloat16)


def solution(mesh):
    in_specs = (P("expert", None), P(), P("expert", None, "hidden"), P("expert", None, "hidden"))
    out_specs = P("expert", None, None, "hidden")
    return jax.shard_map(shards, mesh=mesh, in_specs=in_specs, out_specs=out_specs, check_vma=False)
```

```python
import jax
import jax.numpy as jnp
from jax import lax
from jax.sharding import PartitionSpec as P

TOPK = 8
EXPERTS = 32
SWEEPS = 5
TOK_DEV = 64
CAP = 24


EPS = 1e-06


def dispatch_rows(block_ids, tokens):
    tok_local, topk = block_ids.shape
    flat_ids = block_ids.reshape(-1)
    pairs = flat_ids.shape[0]
    onehot = (flat_ids[:, None] == jnp.arange(EXPERTS, dtype=jnp.int32)[None, :]).astype(jnp.bfloat16)
    earlier = (
        jnp.arange(pairs, dtype=jnp.int32)[:, None] > jnp.arange(pairs, dtype=jnp.int32)[None, :]
    ).astype(jnp.bfloat16)
    before = jnp.dot(earlier, onehot, preferred_element_type=jnp.float32)
    my_rank = jnp.sum(before * onehot.astype(jnp.float32), axis=1).astype(jnp.int32)
    pair_ids = flat_ids.reshape(tok_local, topk)
    pair_rank = my_rank.reshape(tok_local, topk)
    hit = (pair_ids[None, None] == jnp.arange(EXPERTS, dtype=jnp.int32)[:, None, None, None]) & (
        pair_rank[None, None] == jnp.arange(CAP, dtype=jnp.int32)[None, :, None, None]
    )
    select = jnp.any(hit, axis=3).astype(tokens.dtype)
    rows = jnp.einsum("est,td->esd", select, tokens, preferred_element_type=jnp.float32)
    return rows.astype(tokens.dtype)


def hidden_sum(values):
    n = lax.axis_size("hidden")
    total = values
    for shift in range(1, n):
        total = total + lax.ppermute(values, "hidden", [(i, (i + shift) % n) for i in range(n)])
    return total


def row_terms(weight, cols_sq):
    values = weight.astype(jnp.float32)
    return jnp.sum(values * values * cols_sq[:, None, :], axis=2)


def col_terms(weight, scale_sq):
    values = weight.astype(jnp.float32)
    return jnp.sum(values * values * scale_sq[:, :, None], axis=1)


def shards(tokens, expert_ids, gate_weight, up_weight):
    exp_local = gate_weight.shape[0]
    width = gate_weight.shape[1]
    ff_local = gate_weight.shape[2]
    ff_total = ff_local * lax.axis_size("hidden")
    my_index = lax.axis_index("expert")
    tok_local = tokens.shape[0]
    block_ids = lax.dynamic_slice_in_dim(expert_ids, my_index * tok_local, tok_local, 0)
    outgoing = dispatch_rows(block_ids, tokens)
    routed = lax.all_to_all(outgoing, "expert", split_axis=0, concat_axis=0, tiled=True)[None]
    def sweep(_, carry):
        gate_cols, up_cols, _ = carry
        partial_rows = row_terms(gate_weight, gate_cols * gate_cols) + row_terms(
            up_weight, up_cols * up_cols
        )
        row_sums = hidden_sum(partial_rows)
        row_scale = lax.rsqrt(width * row_sums / (2 * ff_total) + EPS)
        scale_sq = row_scale * row_scale
        gate_cols = lax.rsqrt(col_terms(gate_weight, scale_sq) + EPS)
        up_cols = lax.rsqrt(col_terms(up_weight, scale_sq) + EPS)
        return gate_cols, up_cols, row_scale

    carry = (
        jnp.ones((exp_local, ff_local), jnp.float32),
        jnp.ones((exp_local, ff_local), jnp.float32),
        jnp.ones((exp_local, width), jnp.float32),
    )
    gate_cols, up_cols, row_scale = lax.fori_loop(0, SWEEPS, sweep, carry)
    gate_eq = (
        gate_weight.astype(jnp.float32) * row_scale[:, :, None] * gate_cols[:, None, :]
    ).astype(jnp.bfloat16)
    up_eq = (up_weight.astype(jnp.float32) * row_scale[:, :, None] * up_cols[:, None, :]).astype(
        jnp.bfloat16
    )
    both_eq = lax.optimization_barrier(jnp.concatenate([gate_eq, up_eq], axis=2))
    act = jnp.einsum("ensd,edf->ensf", routed, both_eq, preferred_element_type=jnp.float32)
    gate_act = act[..., :ff_local]
    up_act = act[..., ff_local:]
    return (jax.nn.silu(gate_act) * up_act).astype(jnp.bfloat16)


def solution(mesh):
    in_specs = (P("expert", None), P(), P("expert", None, "hidden"), P("expert", None, "hidden"))
    out_specs = P("expert", None, None, "hidden")
    return jax.shard_map(shards, mesh=mesh, in_specs=in_specs, out_specs=out_specs, check_vma=False)
```

```python
import jax
import jax.numpy as jnp
from jax import lax
from jax.sharding import PartitionSpec as P

TOPK = 8
EXPERTS = 32
SWEEPS = 5
TOK_DEV = 64
CAP = 24


EPS = 1e-06


def dispatch_rows(block_ids, tokens):
    tok_local, topk = block_ids.shape
    flat_ids = block_ids.reshape(-1)
    pairs = flat_ids.shape[0]
    onehot = (flat_ids[:, None] == jnp.arange(EXPERTS, dtype=jnp.int32)[None, :]).astype(jnp.bfloat16)
    earlier = (
        jnp.arange(pairs, dtype=jnp.int32)[:, None] > jnp.arange(pairs, dtype=jnp.int32)[None, :]
    ).astype(jnp.bfloat16)
    before = jnp.dot(earlier, onehot, preferred_element_type=jnp.float32)
    my_rank = jnp.sum(before * onehot.astype(jnp.float32), axis=1).astype(jnp.int32)
    pair_ids = flat_ids.reshape(tok_local, topk)
    pair_rank = my_rank.reshape(tok_local, topk)
    hit = (pair_ids[None, None] == jnp.arange(EXPERTS, dtype=jnp.int32)[:, None, None, None]) & (
        pair_rank[None, None] == jnp.arange(CAP, dtype=jnp.int32)[None, :, None, None]
    )
    select = jnp.any(hit, axis=3).astype(tokens.dtype)
    rows = jnp.einsum("est,td->esd", select, tokens, preferred_element_type=jnp.float32)
    return rows.astype(tokens.dtype)


def hidden_sum(values):
    n = lax.axis_size("hidden")
    total = values
    for shift in range(1, n):
        total = total + lax.ppermute(values, "hidden", [(i, (i + shift) % n) for i in range(n)])
    return total


def row_terms(weight, cols_sq):
    values = weight.astype(jnp.float32)
    return jnp.sum(values * values * cols_sq[:, None, :], axis=2)


def col_terms(weight, scale_sq):
    values = weight.astype(jnp.float32)
    return jnp.sum(values * values * scale_sq[:, :, None], axis=1)


def shards(tokens, expert_ids, gate_weight, up_weight):
    exp_local = gate_weight.shape[0]
    width = gate_weight.shape[1]
    ff_local = gate_weight.shape[2]
    ff_total = ff_local * lax.axis_size("hidden")
    my_index = lax.axis_index("expert")
    tok_local = tokens.shape[0]
    block_ids = lax.dynamic_slice_in_dim(expert_ids, my_index * tok_local, tok_local, 0)
    outgoing = dispatch_rows(block_ids, tokens)
    routed = lax.all_to_all(outgoing, "expert", split_axis=0, concat_axis=0, tiled=True)[None]
    def sweep(_, carry):
        gate_cols, up_cols, _ = carry
        partial_rows = row_terms(gate_weight, gate_cols * gate_cols) + row_terms(
            up_weight, up_cols * up_cols
        )
        row_sums = hidden_sum(partial_rows)
        row_scale = lax.rsqrt(width * row_sums / (2 * ff_total) + EPS)
        scale_sq = row_scale * row_scale
        gate_cols = lax.rsqrt(col_terms(gate_weight, scale_sq) + EPS)
        up_cols = lax.rsqrt(col_terms(up_weight, scale_sq) + EPS)
        return gate_cols, up_cols, row_scale

    carry = (
        jnp.ones((exp_local, ff_local), jnp.float32),
        jnp.ones((exp_local, ff_local), jnp.float32),
        jnp.ones((exp_local, width), jnp.float32),
    )
    gate_cols, up_cols, row_scale = lax.fori_loop(0, SWEEPS, sweep, carry)
    gate_eq = (
        gate_weight.astype(jnp.float32) * row_scale[:, :, None] * gate_cols[:, None, :]
    ).astype(jnp.bfloat16)
    up_eq = (up_weight.astype(jnp.float32) * row_scale[:, :, None] * up_cols[:, None, :]).astype(
        jnp.bfloat16
    )
    gate_eq, up_eq = lax.optimization_barrier((gate_eq, up_eq))
    gate_act = jnp.einsum("ensd,edf->ensf", routed, gate_eq, preferred_element_type=jnp.float32)
    up_act = jnp.einsum("ensd,edf->ensf", routed, up_eq, preferred_element_type=jnp.float32)
    return (jax.nn.silu(gate_act) * up_act).astype(jnp.bfloat16)


def solution(mesh):
    in_specs = (P("expert", None), P(), P("expert", None, "hidden"), P("expert", None, "hidden"))
    out_specs = P("expert", None, None, "hidden")
    return jax.shard_map(shards, mesh=mesh, in_specs=in_specs, out_specs=out_specs, check_vma=False)
```

```python
import jax
import jax.numpy as jnp
from jax import lax
from jax.sharding import PartitionSpec as P

TOPK = 8
EXPERTS = 32
SWEEPS = 5
TOK_DEV = 64
CAP = 24


EPS = 1e-06


def dispatch_rows(block_ids, tokens):
    tok_local, topk = block_ids.shape
    flat_ids = block_ids.reshape(-1)
    pairs = flat_ids.shape[0]
    onehot = (flat_ids[:, None] == jnp.arange(EXPERTS, dtype=jnp.int32)[None, :]).astype(jnp.bfloat16)
    earlier = (
        jnp.arange(pairs, dtype=jnp.int32)[:, None] > jnp.arange(pairs, dtype=jnp.int32)[None, :]
    ).astype(jnp.bfloat16)
    before = jnp.dot(earlier, onehot, preferred_element_type=jnp.float32)
    my_rank = jnp.sum(before * onehot.astype(jnp.float32), axis=1).astype(jnp.int32)
    pair_ids = flat_ids.reshape(tok_local, topk).T
    pair_rank = my_rank.reshape(tok_local, topk).T
    hit = (pair_ids[None, None] == jnp.arange(EXPERTS, dtype=jnp.int32)[:, None, None, None]) & (
        pair_rank[None, None] == jnp.arange(CAP, dtype=jnp.int32)[None, :, None, None]
    )
    select = jnp.any(hit, axis=2).astype(tokens.dtype)
    rows = jnp.einsum("est,td->esd", select, tokens, preferred_element_type=jnp.float32)
    return rows.astype(tokens.dtype)


def hidden_sum(values):
    n = lax.axis_size("hidden")
    total = values
    for shift in range(1, n):
        total = total + lax.ppermute(values, "hidden", [(i, (i + shift) % n) for i in range(n)])
    return total


def row_terms(weight, cols_sq):
    values = weight.astype(jnp.float32)
    return jnp.sum(values * values * cols_sq[:, None, :], axis=2)


def col_terms(weight, scale_sq):
    values = weight.astype(jnp.float32)
    return jnp.sum(values * values * scale_sq[:, :, None], axis=1)


def shards(tokens, expert_ids, gate_weight, up_weight):
    exp_local = gate_weight.shape[0]
    width = gate_weight.shape[1]
    ff_local = gate_weight.shape[2]
    ff_total = ff_local * lax.axis_size("hidden")
    my_index = lax.axis_index("expert")
    tok_local = tokens.shape[0]
    block_ids = lax.dynamic_slice_in_dim(expert_ids, my_index * tok_local, tok_local, 0)
    outgoing = dispatch_rows(block_ids, tokens)
    routed = lax.all_to_all(outgoing, "expert", split_axis=0, concat_axis=0, tiled=True)[None]
    def sweep(_, carry):
        gate_cols, up_cols, _ = carry
        partial_rows = row_terms(gate_weight, gate_cols * gate_cols) + row_terms(
            up_weight, up_cols * up_cols
        )
        row_sums = hidden_sum(partial_rows)
        row_scale = lax.rsqrt(width * row_sums / (2 * ff_total) + EPS)
        scale_sq = row_scale * row_scale
        gate_cols = lax.rsqrt(col_terms(gate_weight, scale_sq) + EPS)
        up_cols = lax.rsqrt(col_terms(up_weight, scale_sq) + EPS)
        return gate_cols, up_cols, row_scale

    carry = (
        jnp.ones((exp_local, ff_local), jnp.float32),
        jnp.ones((exp_local, ff_local), jnp.float32),
        jnp.ones((exp_local, width), jnp.float32),
    )
    gate_cols, up_cols, row_scale = lax.fori_loop(0, SWEEPS, sweep, carry)
    gate_eq = (
        gate_weight.astype(jnp.float32) * row_scale[:, :, None] * gate_cols[:, None, :]
    ).astype(jnp.bfloat16)
    up_eq = (up_weight.astype(jnp.float32) * row_scale[:, :, None] * up_cols[:, None, :]).astype(
        jnp.bfloat16
    )
    both_eq = lax.optimization_barrier(jnp.concatenate([gate_eq, up_eq], axis=2))
    act = jnp.einsum("ensd,edf->ensf", routed, both_eq, preferred_element_type=jnp.float32)
    gate_act = act[..., :ff_local]
    up_act = act[..., ff_local:]
    return (jax.nn.silu(gate_act) * up_act).astype(jnp.bfloat16)


def solution(mesh):
    in_specs = (P("expert", None), P(), P("expert", None, "hidden"), P("expert", None, "hidden"))
    out_specs = P("expert", None, None, "hidden")
    return jax.shard_map(shards, mesh=mesh, in_specs=in_specs, out_specs=out_specs, check_vma=False)
```

```python
import jax
import jax.numpy as jnp
from jax import lax
from jax.sharding import PartitionSpec as P

TOPK = 8
EXPERTS = 32
SWEEPS = 5
TOK_DEV = 64
CAP = 24


EPS = 1e-06


def dispatch_rows(block_ids, tokens):
    tok_local, topk = block_ids.shape
    flat_ids = block_ids.reshape(-1)
    pairs = flat_ids.shape[0]
    onehot = (flat_ids[:, None] == jnp.arange(EXPERTS, dtype=jnp.int32)[None, :]).astype(jnp.bfloat16)
    earlier = (
        jnp.arange(pairs, dtype=jnp.int32)[:, None] > jnp.arange(pairs, dtype=jnp.int32)[None, :]
    ).astype(jnp.bfloat16)
    before = jnp.dot(earlier, onehot, preferred_element_type=jnp.float32)
    my_rank = jnp.sum(before * onehot.astype(jnp.float32), axis=1).astype(jnp.int32)
    pair_ids = flat_ids.reshape(tok_local, topk)
    pair_rank = my_rank.reshape(tok_local, topk)
    hit = (pair_ids[None, None] == jnp.arange(EXPERTS, dtype=jnp.int32)[:, None, None, None]) & (
        pair_rank[None, None] == jnp.arange(CAP, dtype=jnp.int32)[None, :, None, None]
    )
    select = jnp.any(hit, axis=3).astype(tokens.dtype)
    rows = jnp.einsum("est,td->esd", select, tokens, preferred_element_type=jnp.float32)
    return rows.astype(tokens.dtype)


def hidden_sum(values):
    n = lax.axis_size("hidden")
    total = values
    for shift in range(1, n):
        total = total + lax.ppermute(values, "hidden", [(i, (i + shift) % n) for i in range(n)])
    return total


def row_terms(weight, cols_sq):
    values = weight.astype(jnp.float32)
    return jnp.sum(values * values * cols_sq[:, None, :], axis=2)


def col_terms(weight, scale_sq):
    values = weight.astype(jnp.float32)
    return jnp.sum(values * values * scale_sq[:, :, None], axis=1)


def shards(tokens, expert_ids, gate_weight, up_weight):
    exp_local = gate_weight.shape[0]
    width = gate_weight.shape[1]
    ff_local = gate_weight.shape[2]
    ff_total = ff_local * lax.axis_size("hidden")
    my_index = lax.axis_index("expert")
    tok_local = tokens.shape[0]
    block_ids = expert_ids.reshape(-1, tok_local, expert_ids.shape[1])[my_index]
    outgoing = dispatch_rows(block_ids, tokens)
    routed = lax.all_to_all(outgoing, "expert", split_axis=0, concat_axis=0, tiled=True)[None]
    def sweep(_, carry):
        gate_cols, up_cols, _ = carry
        partial_rows = row_terms(gate_weight, gate_cols * gate_cols) + row_terms(
            up_weight, up_cols * up_cols
        )
        row_sums = hidden_sum(partial_rows)
        row_scale = lax.rsqrt(width * row_sums / (2 * ff_total) + EPS)
        scale_sq = row_scale * row_scale
        gate_cols = lax.rsqrt(col_terms(gate_weight, scale_sq) + EPS)
        up_cols = lax.rsqrt(col_terms(up_weight, scale_sq) + EPS)
        return gate_cols, up_cols, row_scale

    carry = (
        jnp.ones((exp_local, ff_local), jnp.float32),
        jnp.ones((exp_local, ff_local), jnp.float32),
        jnp.ones((exp_local, width), jnp.float32),
    )
    gate_cols, up_cols, row_scale = lax.fori_loop(0, SWEEPS, sweep, carry)
    gate_eq = (
        gate_weight.astype(jnp.float32) * row_scale[:, :, None] * gate_cols[:, None, :]
    ).astype(jnp.bfloat16)
    up_eq = (up_weight.astype(jnp.float32) * row_scale[:, :, None] * up_cols[:, None, :]).astype(
        jnp.bfloat16
    )
    both_eq = lax.optimization_barrier(jnp.concatenate([gate_eq, up_eq], axis=2))
    act = jnp.einsum("ensd,edf->ensf", routed, both_eq, preferred_element_type=jnp.float32)
    gate_act = act[..., :ff_local]
    up_act = act[..., ff_local:]
    return (jax.nn.silu(gate_act) * up_act).astype(jnp.bfloat16)


def solution(mesh):
    in_specs = (P("expert", None), P(), P("expert", None, "hidden"), P("expert", None, "hidden"))
    out_specs = P("expert", None, None, "hidden")
    return jax.shard_map(shards, mesh=mesh, in_specs=in_specs, out_specs=out_specs, check_vma=False)
```
